256 devices in a mesh: tm: 64 (over z, y, core), ingest: 4 (over x).
Axes of the slice: x: 4, y: 4, z: 8, core: 2. Of those that a mesh axis runs over, the one named last changes fastest.
Arguments:
- trans: float32 [512, 384, 384], P('tm')
- gain: float32 [512, 384, 192], P('tm', None, 'ingest'), may hold values from -0.0048828125 to 0.0048828125
- prior_mean: float32 [384], replicated, may hold values from -8 to 8
- obs_basis: bfloat16 [131072, 192], P(('tm', 'ingest')), may hold values from -6 to 6
- obs_value: float32 [131072], P(('tm', 'ingest')), may hold values from -6 to 6
- measurement_within_tile: int32 [131072], P(('tm', 'ingest')), may hold values from 0 to 7
- observed_row_count: int32 [256, 64], P(('tm', 'ingest')), may hold values from 1 to 8, as said below
Outputs:
- filtered: float32 [512, 384], P('tm')
The draws below stay inside these ranges and needn't reach their ends.
Inputs may be any that keep to these rules, and one draw needn't show every extreme that they name: `observed_row_count`: rows of a group at positions from its count on are not live; every device's row of counts has one group of 8 live rows.
All inputs are finite; a program needn't handle non-finite values.
Results may differ from the reference program's by a relative error of at most 0.0023.
Values may be sent and summed in bfloat16 or wider, within the bound.
No kernel may reach another device: no remote copies, remote signals or barrier semaphores. Data moves between devices by JAX's collectives and lax.ppermute only.
A program may use at most 128 MiB of HBM per device.

```python
import math
import jax
import jax.numpy as jnp
from jax import lax

SB = 192
S = 384
STEP_DEV = 8
OBS_DEV = 512
CAP = 8
EPOCH_LENGTH = 512
MEASURED_ENTRIES = 131072
N_TM = 64
N_INGEST = 4


def draw_trans(key, part):
    stochastic_seeds = jax.random.split(jax.random.fold_in(key, 11), 4)
    incidence_intensity = jnp.exp(jax.random.uniform(stochastic_seeds[0], (S,), minval=math.log(1.0 / (2 * EPOCH_LENGTH)), maxval=math.log(1.0 / 30)))
    noise = jax.random.normal(stochastic_seeds[3], (EPOCH_LENGTH, S, S))
    drifting_baseline = jax.random.uniform(stochastic_seeds[1], (EPOCH_LENGTH, S), minval=0.5, maxval=2.0)
    spike_magnitude = jnp.where(jax.random.uniform(stochastic_seeds[2], (EPOCH_LENGTH, 1)) < 3.0 / EPOCH_LENGTH, 0.6, 1.0)
    damping_multiplier = jnp.exp(-incidence_intensity[None, :] * drifting_baseline) * spike_magnitude * math.exp(-0.02)
    diagonal = jnp.eye(S, dtype=jnp.float32)[None, :, :] * damping_multiplier[:, :, None]
    return (diagonal + noise * (0.2 / math.sqrt(S))).astype(jnp.float32)


def draw_observed_row_count(key, part):
    stochastic_seeds = jax.random.split(jax.random.fold_in(key, 23), 2)
    device_rows = N_TM * N_INGEST
    base = jax.random.randint(stochastic_seeds[0], (device_rows, N_TM), 1, CAP + 1)
    full_group = jax.random.randint(stochastic_seeds[1], (device_rows, 1), 0, N_TM)
    groups = jnp.arange(N_TM, dtype=jnp.int32)[None, :]
    return jnp.where(groups == full_group, CAP, base).astype(jnp.int32)


def touch_ends(array, key, smallest, high):
    extent = array.shape
    spot = [jax.random.randint(jax.random.fold_in(key, axis), (), 0, extent[axis]) for axis in range(len(extent))]
    array = array.at[tuple(spot)].set(smallest)
    longest = extent.index(max(extent))
    spot[longest] = (spot[longest] + 1) % extent[longest]
    return array.at[tuple(spot)].set(high)


def level_of(key, extent, shards, low, largest):
    def one(dim, parts):
        steps = jax.random.uniform(jax.random.fold_in(jax.random.fold_in(key, 6), dim), (parts,), jnp.float32, low / len(shards), largest / len(shards))
        return jnp.repeat(jnp.exp(steps), extent[dim] // parts).reshape((-1,) + (1,) * (len(extent) - dim - 1))

    level = one(*shards[0])
    for cut in shards[1:]:
        level = level * one(*cut)
    return level


def bell_draw(key, dims, scale, reach, pieces=(), kind=jnp.bfloat16):
    entries = jax.random.normal(key, dims, jnp.float32) * scale
    if len(pieces) > 0:
        entries = level_of(key, dims, pieces, -0.22, 0.18) * entries
    return jnp.clip(entries, min=-reach, max=reach).astype(kind)


def setup_inputs(seed: int = 0) -> dict:
    key_of = jax.random.split(jax.random.key(seed), 8)
    trans = draw_trans(jax.random.fold_in(key_of[7], 71), 0)
    gain = bell_draw(key_of[1], (EPOCH_LENGTH, S, SB), (32 * SB * OBS_DEV * N_INGEST // STEP_DEV) ** -0.5, 0.0048828125, ((0, 64), (2, 4)), jnp.float32)
    prior_mean = bell_draw(key_of[2], (S,), 2.0, 8.0, (), jnp.float32)
    obs_basis = bell_draw(key_of[3], (MEASURED_ENTRIES, SB), 1.0, 6.0, ((0, 256),))
    obs_value = bell_draw(key_of[4], (MEASURED_ENTRIES,), 1.0, 6.0, ((0, 256),), jnp.float32)
    measurement_within_tile = touch_ends(jax.random.randint(key_of[5], (MEASURED_ENTRIES,), 0, STEP_DEV), jax.random.fold_in(key_of[5], 1), 0, STEP_DEV - 1).astype(jnp.int32)
    observed_row_count = draw_observed_row_count(jax.random.fold_in(key_of[7], 71), 0)
    return {"trans": trans, "gain": gain, "prior_mean": prior_mean, "obs_basis": obs_basis, "obs_value": obs_value, "measurement_within_tile": measurement_within_tile, "observed_row_count": observed_row_count}


def reference(trans, gain, prior_mean, obs_basis, obs_value, measurement_within_tile, observed_row_count):
    exact = lax.Precision.HIGHEST
    weighted = (obs_basis.astype(jnp.float32) * obs_value[:, None]).astype(jnp.bfloat16)
    row_ids = jnp.arange(obs_basis.shape[0], dtype=jnp.int32)
    source = row_ids // OBS_DEV
    group = (row_ids % OBS_DEV) // CAP
    position = row_ids % CAP
    live_count = observed_row_count[source, group]
    is_live = position < live_count
    step_of = group * STEP_DEV + measurement_within_tile
    live_rows = jnp.where(is_live[:, None], weighted.astype(jnp.float32), jnp.zeros((), jnp.float32))
    drive_sums = jax.ops.segment_sum(live_rows, jnp.where(is_live, step_of, 0).astype(jnp.int32), num_segments=EPOCH_LENGTH)
    forcing = jnp.einsum("tsq,tq->ts", gain, drive_sums, precision=exact)

    def advance(state_mean, inputs):
        step_map, step_force = inputs
        state_mean = jnp.dot(step_map, state_mean, precision=exact) + step_force
        return state_mean, state_mean

    _, filtered = lax.scan(advance, prior_mean, (trans, forcing))
    return filtered
```

```python
import jax
import jax.numpy as jnp
from jax import lax
from jax.sharding import PartitionSpec as P


def passed_along(block, axis, distance):
    devices = range(lax.axis_size(axis))
    route = [(i - distance, i) for i in devices if i - distance in devices]
    return lax.ppermute(block, axis, route)


def on_device(
    trans, gain, prior_mean, obs_basis, obs_value, measurement_within_tile, observed_row_count
):
    exact = lax.Precision.HIGHEST
    tm_count = lax.axis_size("tm")
    in_count = lax.axis_size("ingest")
    steps_here = trans.shape[0]
    state_width = trans.shape[1]
    basis_count = obs_basis.shape[1]
    piece_width = basis_count // in_count
    group_rows = obs_basis.shape[0] // tm_count

    weighted = (obs_basis.astype(jnp.float32) * obs_value[:, None]).astype(jnp.bfloat16)
    pieces = weighted.reshape(tm_count, group_rows, in_count, piece_width)
    pieces = pieces.transpose(0, 2, 1, 3).reshape(tm_count * in_count, group_rows * piece_width)
    is_valid = lax.broadcasted_iota(
        jnp.int32, (tm_count, group_rows), 1
    ) < observed_row_count.reshape(tm_count, 1)
    marked = jnp.where(is_valid, measurement_within_tile.reshape(tm_count, group_rows), -1)
    marks = jnp.broadcast_to(
        marked.astype(jnp.bfloat16)[:, None, :], (tm_count, in_count, group_rows)
    ).reshape(tm_count * in_count, group_rows)
    sent = jnp.concatenate([pieces, marks], axis=1)
    got = lax.all_to_all(sent, ("tm", "ingest"), split_axis=0, concat_axis=0, tiled=True)
    got_rows = got[:, : group_rows * piece_width].reshape(-1, piece_width)
    got_marks = got[:, group_rows * piece_width :].reshape(-1).astype(jnp.int32)
    step_ids = lax.broadcasted_iota(jnp.int32, (1, steps_here), 1)
    onehot = (got_marks[:, None] == step_ids).astype(jnp.bfloat16)
    drive_piece = jnp.einsum("rl,rq->lq", onehot, got_rows, preferred_element_type=jnp.float32)
    partial_force = jnp.einsum("lsq,lq->ls", gain, drive_piece, precision=exact)
    forcing = lax.psum(partial_force, "ingest")

    def compose(prefix, step_map):
        prefix = jnp.dot(step_map, prefix, precision=exact)
        return prefix, prefix

    _, prefix_maps = lax.scan(compose, jnp.eye(state_width, dtype=jnp.float32), trans)

    def advance(offset, inputs):
        step_map, step_force = inputs
        offset = jnp.dot(step_map, offset, precision=exact) + step_force
        return offset, offset

    _, offsets = lax.scan(advance, jnp.zeros((state_width,), jnp.float32), (trans, forcing))

    tm_index = lax.axis_index("tm")
    is_first = tm_index == 0
    slab_map = prefix_maps[-1]
    acc_vec = jnp.where(
        is_first, jnp.dot(slab_map, prior_mean, precision=exact) + offsets[-1], offsets[-1]
    )
    acc_map = jnp.where(is_first, jnp.zeros_like(slab_map), slab_map)
    distance = 1
    while distance < tm_count:
        got_vec = passed_along(acc_vec, "tm", distance)
        last = distance * 2 >= tm_count
        if not last:
            got_map = passed_along(acc_map, "tm", distance)
        acc_vec = jnp.dot(acc_map, got_vec, precision=exact) + acc_vec
        if not last:
            acc_map = jnp.dot(acc_map, got_map, precision=exact)
        distance *= 2
    entering = jnp.where(is_first, prior_mean, passed_along(acc_vec, "tm", 1))
    filtered = jnp.einsum("lsq,q->ls", prefix_maps, entering, precision=exact) + offsets
    return filtered


def solution(mesh):
    return jax.shard_map(
        on_device,
        mesh=mesh,
        in_specs=(
            P("tm", None, None),
            P("tm", None, "ingest"),
            P(),
            P(("tm", "ingest"), None),
            P(("tm", "ingest")),
            P(("tm", "ingest")),
            P(("tm", "ingest"), None),
        ),
        out_specs=P("tm", None),
        check_vma=False,
    )
```

```python
import jax
import jax.numpy as jnp
from jax import lax
from jax.sharding import PartitionSpec as P


def passed_along(block, axis, distance):
    devices = range(lax.axis_size(axis))
    route = [(i - distance, i) for i in devices if i - distance in devices]
    return lax.ppermute(block, axis, route)


def summed_over(block, axis):
    distance = 1
    while distance < lax.axis_size(axis):
        route = [(i, i ^ distance) for i in range(lax.axis_size(axis))]
        block = block + lax.ppermute(block, axis, route)
        distance *= 2
    return block


def on_device(
    trans, gain, prior_mean, obs_basis, obs_value, measurement_within_tile, observed_row_count
):
    exact = lax.Precision.HIGHEST
    tm_count = lax.axis_size("tm")
    in_count = lax.axis_size("ingest")
    steps_here = trans.shape[0]
    state_width = trans.shape[1]
    basis_count = obs_basis.shape[1]
    piece_width = basis_count // in_count
    group_rows = obs_basis.shape[0] // tm_count

    weighted = (obs_basis.astype(jnp.float32) * obs_value[:, None]).astype(jnp.bfloat16)
    pieces = weighted.reshape(tm_count, group_rows, in_count, piece_width)
    pieces = pieces.transpose(0, 2, 1, 3).reshape(tm_count * in_count, group_rows * piece_width)
    is_valid = lax.broadcasted_iota(
        jnp.int32, (tm_count, group_rows), 1
    ) < observed_row_count.reshape(tm_count, 1)
    marked = jnp.where(is_valid, measurement_within_tile.reshape(tm_count, group_rows), -1)
    marks = jnp.broadcast_to(
        marked.astype(jnp.bfloat16)[:, None, :], (tm_count, in_count, group_rows)
    ).reshape(tm_count * in_count, group_rows)
    sent = jnp.concatenate([pieces, marks], axis=1)
    got = lax.all_to_all(sent, ("tm", "ingest"), split_axis=0, concat_axis=0, tiled=True)
    got_rows = got[:, : group_rows * piece_width].reshape(-1, piece_width)
    got_marks = got[:, group_rows * piece_width :].reshape(-1).astype(jnp.int32)
    step_ids = lax.broadcasted_iota(jnp.int32, (1, steps_here), 1)
    onehot = (got_marks[:, None] == step_ids).astype(jnp.bfloat16)
    drive_piece = jnp.einsum("rl,rq->lq", onehot, got_rows, preferred_element_type=jnp.float32)
    partial_force = jnp.einsum("lsq,lq->ls", gain, drive_piece, precision=exact)
    forcing = summed_over(partial_force, "ingest")

    level = trans
    while level.shape[0] > 1:
        pairs = level.reshape(level.shape[0] // 2, 2, state_width, state_width)
        level = jnp.einsum("jab,jbc->jac", pairs[:, 1], pairs[:, 0], precision=exact)
    slab_map = level[0]
    offset = forcing[0]
    for step in range(1, steps_here):
        offset = jnp.dot(trans[step], offset, precision=exact) + forcing[step]

    tm_index = lax.axis_index("tm")
    is_first = tm_index == 0
    acc_vec = jnp.where(is_first, jnp.dot(slab_map, prior_mean, precision=exact) + offset, offset)
    acc_map = jnp.where(is_first, jnp.zeros_like(slab_map), slab_map)
    distance = 1
    while distance < tm_count:
        got_vec = passed_along(acc_vec, "tm", distance)
        last = distance * 2 >= tm_count
        if not last:
            got_map = passed_along(acc_map, "tm", distance)
        acc_vec = jnp.dot(acc_map, got_vec, precision=exact) + acc_vec
        if not last:
            acc_map = jnp.dot(acc_map, got_map, precision=exact)
        distance *= 2
    state = jnp.where(is_first, prior_mean, passed_along(acc_vec, "tm", 1))
    means = []
    for step in range(steps_here):
        state = jnp.dot(trans[step], state, precision=exact) + forcing[step]
        means.append(state)
    return jnp.stack(means)


def solution(mesh):
    return jax.shard_map(
        on_device,
        mesh=mesh,
        in_specs=(
            P("tm", None, None),
            P("tm", None, "ingest"),
            P(),
            P(("tm", "ingest"), None),
            P(("tm", "ingest")),
            P(("tm", "ingest")),
            P(("tm", "ingest"), None),
        ),
        out_specs=P("tm", None),
        check_vma=False,
    )
```

```python
import jax
import jax.numpy as jnp
from jax import lax
from jax.sharding import PartitionSpec as P


def passed_along(block, axis, distance):
    devices = range(lax.axis_size(axis))
    route = [(i - distance, i) for i in devices if i - distance in devices]
    return lax.ppermute(block, axis, route)


def summed_over(block, axis):
    count = lax.axis_size(axis)
    shares = [block] + [
        lax.ppermute(block, axis, [(i, (i + shift) % count) for i in range(count)])
        for shift in range(1, count)
    ]
    by_source = jnp.stack(shares)[(lax.axis_index(axis) - jnp.arange(count)) % count]
    total = by_source[0]
    for source in range(1, count):
        total = total + by_source[source]
    return total


def on_device(
    trans, gain, prior_mean, obs_basis, obs_value, measurement_within_tile, observed_row_count
):
    exact = lax.Precision.HIGHEST
    tm_count = lax.axis_size("tm")
    in_count = lax.axis_size("ingest")
    steps_here = trans.shape[0]
    state_width = trans.shape[1]
    basis_count = obs_basis.shape[1]
    piece_width = basis_count // in_count
    group_rows = obs_basis.shape[0] // tm_count

    weighted = (obs_basis.astype(jnp.float32) * obs_value[:, None]).astype(jnp.bfloat16)
    pieces = weighted.reshape(tm_count, group_rows, in_count, piece_width)
    pieces = pieces.transpose(0, 2, 1, 3).reshape(tm_count * in_count, group_rows * piece_width)
    is_valid = lax.broadcasted_iota(
        jnp.int32, (tm_count, group_rows), 1
    ) < observed_row_count.reshape(tm_count, 1)
    marked = jnp.where(is_valid, measurement_within_tile.reshape(tm_count, group_rows), -1)
    marks = jnp.broadcast_to(
        marked.astype(jnp.bfloat16)[:, None, :], (tm_count, in_count, group_rows)
    ).reshape(tm_count * in_count, group_rows)
    sent = jnp.concatenate([pieces, marks], axis=1)
    got = lax.all_to_all(sent, ("tm", "ingest"), split_axis=0, concat_axis=0, tiled=True)
    got_rows = got[:, : group_rows * piece_width].reshape(-1, piece_width)
    got_marks = got[:, group_rows * piece_width :].reshape(-1).astype(jnp.int32)
    step_ids = lax.broadcasted_iota(jnp.int32, (1, steps_here), 1)
    onehot = (got_marks[:, None] == step_ids).astype(jnp.bfloat16)
    drive_piece = jnp.einsum("rl,rq->lq", onehot, got_rows, preferred_element_type=jnp.float32)
    partial_force = jnp.einsum("lsq,lq->ls", gain, drive_piece, precision=exact)
    forcing = summed_over(partial_force, "ingest")

    level = trans
    while level.shape[0] > 1:
        pairs = level.reshape(level.shape[0] // 2, 2, state_width, state_width)
        level = jnp.einsum("jab,jbc->jac", pairs[:, 1], pairs[:, 0], precision=exact)
    slab_map = level[0]
    offset = forcing[0]
    for step in range(1, steps_here):
        offset = jnp.dot(trans[step], offset, precision=exact) + forcing[step]

    tm_index = lax.axis_index("tm")
    is_first = tm_index == 0
    acc_vec = jnp.where(is_first, jnp.dot(slab_map, prior_mean, precision=exact) + offset, offset)
    acc_map = jnp.where(is_first, jnp.zeros_like(slab_map), slab_map)
    distance = 1
    history = [acc_vec]
    while distance < tm_count:
        last = distance * 2 >= tm_count
        if len(history) >= 3 and not last:
            acc_map, _ = lax.optimization_barrier((acc_map, history[-3]))
        got_vec = passed_along(acc_vec, "tm", distance)
        if not last:
            got_map = passed_along(acc_map, "tm", distance)
        acc_vec = jnp.dot(acc_map, got_vec, precision=exact) + acc_vec
        if not last:
            acc_map = jnp.dot(acc_map, got_map, precision=exact)
        history.append(acc_vec)
        distance *= 2
    state = jnp.where(is_first, prior_mean, passed_along(acc_vec, "tm", 1))
    means = []
    for step in range(steps_here):
        state = jnp.dot(trans[step], state, precision=exact) + forcing[step]
        means.append(state)
    return jnp.stack(means)


def solution(mesh):
    return jax.shard_map(
        on_device,
        mesh=mesh,
        in_specs=(
            P("tm", None, None),
            P("tm", None, "ingest"),
            P(),
            P(("tm", "ingest"), None),
            P(("tm", "ingest")),
            P(("tm", "ingest")),
            P(("tm", "ingest"), None),
        ),
        out_specs=P("tm", None),
        check_vma=False,
    )
```

```python
import jax
import jax.numpy as jnp
from jax import lax
from jax.sharding import PartitionSpec as P


def passed_along(block, axis, distance):
    devices = range(lax.axis_size(axis))
    route = [(i - distance, i) for i in devices if i - distance in devices]
    return lax.ppermute(block, axis, route)


def summed_over(block, axis):
    count = lax.axis_size(axis)
    shares = [block] + [
        lax.ppermute(block, axis, [(i, (i + shift) % count) for i in range(count)])
        for shift in range(1, count)
    ]
    by_source = jnp.stack(shares)[(lax.axis_index(axis) - jnp.arange(count)) % count]
    total = by_source[0]
    for source in range(1, count):
        total = total + by_source[source]
    return total


def on_device(
    trans, gain, prior_mean, obs_basis, obs_value, measurement_within_tile, observed_row_count
):
    exact = lax.Precision.HIGHEST
    tm_count = lax.axis_size("tm")
    in_count = lax.axis_size("ingest")
    steps_here = trans.shape[0]
    state_width = trans.shape[1]
    basis_count = obs_basis.shape[1]
    piece_width = basis_count // in_count
    group_rows = obs_basis.shape[0] // tm_count

    weighted = (obs_basis.astype(jnp.float32) * obs_value[:, None]).astype(jnp.bfloat16)
    pieces = weighted.reshape(tm_count, group_rows, in_count, piece_width)
    pieces = pieces.transpose(0, 2, 1, 3).reshape(tm_count * in_count, group_rows * piece_width)
    is_valid = lax.broadcasted_iota(
        jnp.int32, (tm_count, group_rows), 1
    ) < observed_row_count.reshape(tm_count, 1)
    marked = jnp.where(is_valid, measurement_within_tile.reshape(tm_count, group_rows), -1)
    marks = jnp.broadcast_to(
        marked.astype(jnp.bfloat16)[:, None, :], (tm_count, in_count, group_rows)
    ).reshape(tm_count * in_count, group_rows)
    sent = jnp.concatenate([pieces, marks], axis=1)
    got = lax.all_to_all(sent, ("tm", "ingest"), split_axis=0, concat_axis=0, tiled=True)
    got_rows = got[:, : group_rows * piece_width].reshape(-1, piece_width)
    got_marks = got[:, group_rows * piece_width :].reshape(-1).astype(jnp.int32)
    step_ids = lax.broadcasted_iota(jnp.int32, (1, steps_here), 1)
    onehot = (got_marks[:, None] == step_ids).astype(jnp.bfloat16)
    drive_piece = jnp.einsum("rl,rq->lq", onehot, got_rows, preferred_element_type=jnp.float32)
    partial_force = jnp.einsum("lsq,lq->ls", gain, drive_piece, precision=exact)
    forcing = summed_over(partial_force, "ingest")

    pairs = trans.reshape(steps_here // 2, 2, state_width, state_width)
    force_pairs = forcing.reshape(steps_here // 2, 2, state_width)
    level_t = jnp.einsum("jba,jcb->jac", pairs[:, 0], pairs[:, 1], precision=exact)
    level_off = (
        jnp.einsum("jab,jb->ja", pairs[:, 1], force_pairs[:, 0], precision=exact)
        + force_pairs[:, 1]
    )
    while level_t.shape[0] > 1:
        map_pairs = level_t.reshape(-1, 2, state_width, state_width)
        off_pairs = level_off.reshape(-1, 2, state_width)
        level_off = (
            jnp.einsum("ja,jab->jb", off_pairs[:, 0], map_pairs[:, 1], precision=exact)
            + off_pairs[:, 1]
        )
        level_t = jnp.einsum("jab,jbc->jac", map_pairs[:, 0], map_pairs[:, 1], precision=exact)
    slab_t = level_t[0]
    offset = level_off[0]

    tm_index = lax.axis_index("tm")
    is_first = tm_index == 0
    acc_vec = jnp.where(is_first, jnp.dot(prior_mean, slab_t, precision=exact) + offset, offset)
    acc_t = jnp.where(is_first, jnp.zeros_like(slab_t), slab_t)
    distance = 1
    while distance < tm_count:
        if distance * 2 >= tm_count:
            got_vec = passed_along(acc_vec, "tm", distance)
            acc_vec = jnp.dot(got_vec, acc_t, precision=exact) + acc_vec
        elif distance < 4:
            got_vec = passed_along(acc_vec, "tm", distance)
            got_t = passed_along(acc_t, "tm", distance)
            acc_vec = jnp.dot(got_vec, acc_t, precision=exact) + acc_vec
            acc_t = jnp.dot(got_t, acc_t, precision=exact)
        else:
            carried = jnp.concatenate([acc_t, acc_vec[None]], axis=0)
            got = jnp.dot(passed_along(carried, "tm", distance), acc_t, precision=exact)
            acc_t = got[:state_width]
            acc_vec = got[state_width] + acc_vec
        distance *= 2
    state = jnp.where(is_first, prior_mean, passed_along(acc_vec, "tm", 1))
    means = []
    for step in range(steps_here):
        state = jnp.dot(trans[step], state, precision=exact) + forcing[step]
        means.append(state)
    return jnp.stack(means)


def solution(mesh):
    return jax.shard_map(
        on_device,
        mesh=mesh,
        in_specs=(
            P("tm", None, None),
            P("tm", None, "ingest"),
            P(),
            P(("tm", "ingest"), None),
            P(("tm", "ingest")),
            P(("tm", "ingest")),
            P(("tm", "ingest"), None),
        ),
        out_specs=P("tm", None),
        check_vma=False,
    )
```

```python
import jax
import jax.numpy as jnp
from jax import lax
from jax.sharding import PartitionSpec as P


def passed_along(block, axis, distance):
    devices = range(lax.axis_size(axis))
    route = [(i - distance, i) for i in devices if i - distance in devices]
    return lax.ppermute(block, axis, route)


def summed_over(block, axis):
    count = lax.axis_size(axis)
    shares = [block] + [
        lax.ppermute(block, axis, [(i, (i + shift) % count) for i in range(count)])
        for shift in range(1, count)
    ]
    by_source = jnp.stack(shares)[(lax.axis_index(axis) - jnp.arange(count)) % count]
    total = by_source[0]
    for source in range(1, count):
        total = total + by_source[source]
    return total


def on_device(
    trans, gain, prior_mean, obs_basis, obs_value, measurement_within_tile, observed_row_count
):
    exact = lax.Precision.HIGHEST
    tm_count = lax.axis_size("tm")
    in_count = lax.axis_size("ingest")
    steps_here = trans.shape[0]
    state_width = trans.shape[1]
    basis_count = obs_basis.shape[1]
    piece_width = basis_count // in_count
    group_rows = obs_basis.shape[0] // tm_count

    weighted = (obs_basis.astype(jnp.float32) * obs_value[:, None]).astype(jnp.bfloat16)
    pieces = weighted.reshape(tm_count, group_rows, in_count, piece_width)
    pieces = pieces.transpose(0, 2, 1, 3).reshape(tm_count * in_count, group_rows * piece_width)
    is_valid = lax.broadcasted_iota(
        jnp.int32, (tm_count, group_rows), 1
    ) < observed_row_count.reshape(tm_count, 1)
    marked = jnp.where(is_valid, measurement_within_tile.reshape(tm_count, group_rows), -1)
    marks = jnp.broadcast_to(
        marked.astype(jnp.bfloat16)[:, None, :], (tm_count, in_count, group_rows)
    ).reshape(tm_count * in_count, group_rows)
    sent = jnp.concatenate([pieces, marks], axis=1)
    level = trans
    while level.shape[0] > 1:
        pairs = level.reshape(level.shape[0] // 2, 2, state_width, state_width)
        level = jnp.einsum("jab,jbc->jac", pairs[:, 1], pairs[:, 0], precision=exact)
    slab_map = level[0]
    sent, slab_map = lax.optimization_barrier((sent, slab_map))
    got = lax.all_to_all(sent, ("tm", "ingest"), split_axis=0, concat_axis=0, tiled=True)
    got_rows = got[:, : group_rows * piece_width].reshape(-1, piece_width)
    got_marks = got[:, group_rows * piece_width :].reshape(-1).astype(jnp.int32)
    step_ids = lax.broadcasted_iota(jnp.int32, (1, steps_here), 1)
    onehot = (got_marks[:, None] == step_ids).astype(jnp.bfloat16)
    drive_piece = jnp.einsum("rl,rq->lq", onehot, got_rows, preferred_element_type=jnp.float32)
    partial_force = jnp.einsum("lsq,lq->ls", gain, drive_piece, precision=exact)
    forcing = summed_over(partial_force, "ingest")

    offset = forcing[0]
    for step in range(1, steps_here):
        offset = jnp.dot(trans[step], offset, precision=exact) + forcing[step]

    tm_index = lax.axis_index("tm")
    is_first = tm_index == 0
    acc_vec = jnp.where(is_first, jnp.dot(slab_map, prior_mean, precision=exact) + offset, offset)
    acc_map = jnp.where(is_first, jnp.zeros_like(slab_map), slab_map)
    distance = 1
    while distance < tm_count:
        got_vec = passed_along(acc_vec, "tm", distance)
        last = distance * 2 >= tm_count
        if not last:
            got_map = passed_along(acc_map, "tm", distance)
        acc_vec = jnp.dot(acc_map, got_vec, precision=exact) + acc_vec
        if not last:
            acc_map = jnp.dot(acc_map, got_map, precision=exact)
        distance *= 2
    state = jnp.where(is_first, prior_mean, passed_along(acc_vec, "tm", 1))
    means = []
    for step in range(steps_here):
        state = jnp.dot(trans[step], state, precision=exact) + forcing[step]
        means.append(state)
    return jnp.stack(means)


def solution(mesh):
    return jax.shard_map(
        on_device,
        mesh=mesh,
        in_specs=(
            P("tm", None, None),
            P("tm", None, "ingest"),
            P(),
            P(("tm", "ingest"), None),
            P(("tm", "ingest")),
            P(("tm", "ingest")),
            P(("tm", "ingest"), None),
        ),
        out_specs=P("tm", None),
        check_vma=False,
    )
```

```python
import jax
import jax.numpy as jnp
from jax import lax
from jax.sharding import PartitionSpec as P


def passed_along(block, axis, distance):
    devices = range(lax.axis_size(axis))
    route = [(i - distance, i) for i in devices if i - distance in devices]
    return lax.ppermute(block, axis, route)


def summed_over(block, axis):
    count = lax.axis_size(axis)
    shares = [block] + [
        lax.ppermute(block, axis, [(i, (i + shift) % count) for i in range(count)])
        for shift in range(1, count)
    ]
    by_source = jnp.stack(shares)[(lax.axis_index(axis) - jnp.arange(count)) % count]
    total = by_source[0]
    for source in range(1, count):
        total = total + by_source[source]
    return total


def on_device(
    trans, gain, prior_mean, obs_basis, obs_value, measurement_within_tile, observed_row_count
):
    exact = lax.Precision.HIGHEST
    tm_count = lax.axis_size("tm")
    in_count = lax.axis_size("ingest")
    steps_here = trans.shape[0]
    state_width = trans.shape[1]
    basis_count = obs_basis.shape[1]
    piece_width = basis_count // in_count
    group_rows = obs_basis.shape[0] // tm_count

    weighted = (obs_basis.astype(jnp.float32) * obs_value[:, None]).astype(jnp.bfloat16)
    pieces = weighted.reshape(tm_count, group_rows, in_count, piece_width)
    pieces = pieces.transpose(0, 2, 1, 3).reshape(tm_count * in_count, group_rows * piece_width)
    is_valid = lax.broadcasted_iota(
        jnp.int32, (tm_count, group_rows), 1
    ) < observed_row_count.reshape(tm_count, 1)
    marked = jnp.where(is_valid, measurement_within_tile.reshape(tm_count, group_rows), -1)
    marks = jnp.broadcast_to(
        marked.astype(jnp.bfloat16)[:, None, :], (tm_count, in_count, group_rows)
    ).reshape(tm_count * in_count, group_rows)
    sent = jnp.concatenate([pieces, marks], axis=1)
    got = lax.all_to_all(sent, ("tm", "ingest"), split_axis=0, concat_axis=0, tiled=True)
    got_rows = got[:, : group_rows * piece_width].reshape(-1, piece_width)
    got_marks = got[:, group_rows * piece_width :].reshape(-1).astype(jnp.int32)
    step_ids = lax.broadcasted_iota(jnp.int32, (1, steps_here), 1)
    onehot = (got_marks[:, None] == step_ids).astype(jnp.bfloat16)
    drive_piece = jnp.einsum("rl,rq->lq", onehot, got_rows, preferred_element_type=jnp.float32)
    partial_force = jnp.einsum("lsq,lq->ls", gain, drive_piece, precision=exact)
    forcing = summed_over(partial_force, "ingest")

    pairs = trans.reshape(steps_here // 2, 2, state_width, state_width)
    level_t = jnp.einsum("jba,jcb->jac", pairs[:, 0], pairs[:, 1], precision=exact)
    while level_t.shape[0] > 1:
        map_pairs = level_t.reshape(-1, 2, state_width, state_width)
        level_t = jnp.einsum("jab,jbc->jac", map_pairs[:, 0], map_pairs[:, 1], precision=exact)
    slab_t = level_t[0]
    offset = forcing[0]
    for step in range(1, steps_here):
        offset = jnp.dot(trans[step], offset, precision=exact) + forcing[step]

    tm_index = lax.axis_index("tm")
    is_first = tm_index == 0
    acc_vec = jnp.where(is_first, jnp.dot(prior_mean, slab_t, precision=exact) + offset, offset)
    acc_t = jnp.where(is_first, jnp.zeros_like(slab_t), slab_t)
    distance = 1
    while distance < tm_count:
        if distance * 2 >= tm_count:
            got_vec = passed_along(acc_vec, "tm", distance)
            acc_vec = jnp.dot(got_vec, acc_t, precision=exact) + acc_vec
        else:
            carried = jnp.concatenate([acc_t, acc_vec[None]], axis=0)
            got = jnp.dot(passed_along(carried, "tm", distance), acc_t, precision=exact)
            acc_t = got[:state_width]
            acc_vec = got[state_width] + acc_vec
        distance *= 2
    state = jnp.where(is_first, prior_mean, passed_along(acc_vec, "tm", 1))
    means = []
    for step in range(steps_here):
        state = jnp.dot(trans[step], state, precision=exact) + forcing[step]
        means.append(state)
    return jnp.stack(means)


def solution(mesh):
    return jax.shard_map(
        on_device,
        mesh=mesh,
        in_specs=(
            P("tm", None, None),
            P("tm", None, "ingest"),
            P(),
            P(("tm", "ingest"), None),
            P(("tm", "ingest")),
            P(("tm", "ingest")),
            P(("tm", "ingest"), None),
        ),
        out_specs=P("tm", None),
        check_vma=False,
    )
```

```python
import jax
import jax.numpy as jnp
from jax import lax
from jax.experimental import pallas as pl
from jax.experimental.pallas import tpu as pltpu
from jax.sharding import PartitionSpec as P


def passed_along(block, axis, distance):
    devices = range(lax.axis_size(axis))
    route = [(i - distance, i) for i in devices if i - distance in devices]
    return lax.ppermute(block, axis, route)


def summed_over(block, axis):
    count = lax.axis_size(axis)
    shares = [block] + [
        lax.ppermute(block, axis, [(i, (i + shift) % count) for i in range(count)])
        for shift in range(1, count)
    ]
    by_source = jnp.stack(shares)[(lax.axis_index(axis) - jnp.arange(count)) % count]
    total = by_source[0]
    for source in range(1, count):
        total = total + by_source[source]
    return total


def recurrence_kernel(map_ref, force_ref, start_ref, out_ref, state_ref):
    step = pl.program_id(0)

    @pl.when(step == 0)
    def _():
        state_ref[...] = jnp.broadcast_to(start_ref[...], state_ref.shape)

    moved = lax.dot_general(
        state_ref[...],
        map_ref[0],
        (((1,), (1,)), ((), ())),
        precision=lax.Precision.HIGHEST,
        preferred_element_type=jnp.float32,
    )
    state = moved + force_ref[pl.ds(step, 1), :]
    state_ref[...] = state
    out_ref[pl.ds(step, 1), :] = state[0:1, :]


def run_recurrence(trans, forcing, start):
    steps, width = forcing.shape
    return pl.pallas_call(
        recurrence_kernel,
        grid=(steps,),
        in_specs=[
            pl.BlockSpec((1, width, width), lambda t: (t, 0, 0)),
            pl.BlockSpec((steps, width), lambda t: (0, 0)),
            pl.BlockSpec((1, width), lambda t: (0, 0)),
        ],
        out_specs=pl.BlockSpec((steps, width), lambda t: (0, 0)),
        out_shape=jax.ShapeDtypeStruct((steps, width), jnp.float32),
        scratch_shapes=[pltpu.VMEM((8, width), jnp.float32)],
    )(trans, forcing, start.reshape(1, width))


def on_device(
    trans, gain, prior_mean, obs_basis, obs_value, measurement_within_tile, observed_row_count
):
    exact = lax.Precision.HIGHEST
    tm_count = lax.axis_size("tm")
    in_count = lax.axis_size("ingest")
    steps_here = trans.shape[0]
    state_width = trans.shape[1]
    basis_count = obs_basis.shape[1]
    piece_width = basis_count // in_count
    group_rows = obs_basis.shape[0] // tm_count

    weighted = (obs_basis.astype(jnp.float32) * obs_value[:, None]).astype(jnp.bfloat16)
    pieces = weighted.reshape(tm_count, group_rows, in_count, piece_width)
    pieces = pieces.transpose(0, 2, 1, 3).reshape(tm_count * in_count, group_rows * piece_width)
    is_valid = lax.broadcasted_iota(
        jnp.int32, (tm_count, group_rows), 1
    ) < observed_row_count.reshape(tm_count, 1)
    marked = jnp.where(is_valid, measurement_within_tile.reshape(tm_count, group_rows), -1)
    marks = jnp.broadcast_to(
        marked.astype(jnp.bfloat16)[:, None, :], (tm_count, in_count, group_rows)
    ).reshape(tm_count * in_count, group_rows)
    sent = jnp.concatenate([pieces, marks], axis=1)
    got = lax.all_to_all(sent, ("tm", "ingest"), split_axis=0, concat_axis=0, tiled=True)
    got_rows = got[:, : group_rows * piece_width].reshape(-1, piece_width)
    got_marks = got[:, group_rows * piece_width :].reshape(-1).astype(jnp.int32)
    step_ids = lax.broadcasted_iota(jnp.int32, (1, steps_here), 1)
    onehot = (got_marks[:, None] == step_ids).astype(jnp.bfloat16)
    drive_piece = jnp.einsum("rl,rq->lq", onehot, got_rows, preferred_element_type=jnp.float32)
    partial_force = jnp.einsum("lsq,lq->ls", gain, drive_piece, precision=exact)
    forcing = summed_over(partial_force, "ingest")

    pairs = trans.reshape(steps_here // 2, 2, state_width, state_width)
    level_t = jnp.einsum("jba,jcb->jac", pairs[:, 0], pairs[:, 1], precision=exact)
    while level_t.shape[0] > 1:
        map_pairs = level_t.reshape(-1, 2, state_width, state_width)
        level_t = jnp.einsum("jab,jbc->jac", map_pairs[:, 0], map_pairs[:, 1], precision=exact)
    slab_t = level_t[0]
    offset = run_recurrence(trans, forcing, jnp.zeros((state_width,), jnp.float32))[-1]

    tm_index = lax.axis_index("tm")
    is_first = tm_index == 0
    acc_vec = jnp.where(is_first, jnp.dot(prior_mean, slab_t, precision=exact) + offset, offset)
    acc_t = jnp.where(is_first, jnp.zeros_like(slab_t), slab_t)
    distance = 1
    while distance < tm_count:
        if distance * 2 >= tm_count:
            got_vec = passed_along(acc_vec, "tm", distance)
            acc_vec = jnp.dot(got_vec, acc_t, precision=exact) + acc_vec
        else:
            carried = jnp.concatenate([acc_t, acc_vec[None]], axis=0)
            got = jnp.dot(passed_along(carried, "tm", distance), acc_t, precision=exact)
            acc_t = got[:state_width]
            acc_vec = got[state_width] + acc_vec
        distance *= 2
    state = jnp.where(is_first, prior_mean, passed_along(acc_vec, "tm", 1))
    return run_recurrence(trans, forcing, state)


def solution(mesh):
    return jax.shard_map(
        on_device,
        mesh=mesh,
        in_specs=(
            P("tm", None, None),
            P("tm", None, "ingest"),
            P(),
            P(("tm", "ingest"), None),
            P(("tm", "ingest")),
            P(("tm", "ingest")),
            P(("tm", "ingest"), None),
        ),
        out_specs=P("tm", None),
        check_vma=False,
    )
```

```python
import jax
import jax.numpy as jnp
from jax import lax
from jax.experimental import pallas as pl
from jax.experimental.pallas import tpu as pltpu
from jax.sharding import PartitionSpec as P


def passed_along(block, axis, distance):
    devices = range(lax.axis_size(axis))
    route = [(i - distance, i) for i in devices if i - distance in devices]
    return lax.ppermute(block, axis, route)


def summed_over(block, axis):
    count = lax.axis_size(axis)
    shares = [block] + [
        lax.ppermute(block, axis, [(i, (i + shift) % count) for i in range(count)])
        for shift in range(1, count)
    ]
    by_source = jnp.stack(shares)[(lax.axis_index(axis) - jnp.arange(count)) % count]
    total = by_source[0]
    for source in range(1, count):
        total = total + by_source[source]
    return total


def recurrence_kernel(map_ref, force_ref, start_ref, out_ref, state_ref):
    step = pl.program_id(0)

    @pl.when(step == 0)
    def _():
        state_ref[...] = jnp.broadcast_to(start_ref[...], state_ref.shape)

    moved = lax.dot_general(
        state_ref[...],
        map_ref[0],
        (((1,), (1,)), ((), ())),
        precision=lax.Precision.HIGHEST,
        preferred_element_type=jnp.float32,
    )
    state = moved + force_ref[pl.ds(step, 1), :]
    state_ref[...] = state
    out_ref[pl.ds(step, 1), :] = state[0:1, :]


def run_recurrence(trans, forcing, start):
    steps, width = forcing.shape
    return pl.pallas_call(
        recurrence_kernel,
        grid=(steps,),
        in_specs=[
            pl.BlockSpec((1, width, width), lambda t: (t, 0, 0)),
            pl.BlockSpec((steps, width), lambda t: (0, 0)),
            pl.BlockSpec((1, width), lambda t: (0, 0)),
        ],
        out_specs=pl.BlockSpec((steps, width), lambda t: (0, 0)),
        out_shape=jax.ShapeDtypeStruct((steps, width), jnp.float32),
        scratch_shapes=[pltpu.VMEM((8, width), jnp.float32)],
    )(trans, forcing, start.reshape(1, width))


def on_device(
    trans, gain, prior_mean, obs_basis, obs_value, measurement_within_tile, observed_row_count
):
    exact = lax.Precision.HIGHEST
    tm_count = lax.axis_size("tm")
    in_count = lax.axis_size("ingest")
    steps_here = trans.shape[0]
    state_width = trans.shape[1]
    basis_count = obs_basis.shape[1]
    piece_width = basis_count // in_count
    group_rows = obs_basis.shape[0] // tm_count

    weighted = (obs_basis.astype(jnp.float32) * obs_value[:, None]).astype(jnp.bfloat16)
    pieces = weighted.reshape(tm_count, group_rows, in_count, piece_width)
    pieces = pieces.transpose(0, 2, 1, 3).reshape(tm_count * in_count, group_rows * piece_width)
    is_valid = lax.broadcasted_iota(
        jnp.int32, (tm_count, group_rows), 1
    ) < observed_row_count.reshape(tm_count, 1)
    marked = jnp.where(is_valid, measurement_within_tile.reshape(tm_count, group_rows), -1)
    marks = jnp.broadcast_to(
        marked.astype(jnp.bfloat16)[:, None, :], (tm_count, in_count, group_rows)
    ).reshape(tm_count * in_count, group_rows)
    sent = jnp.concatenate([pieces, marks], axis=1)
    got = lax.all_to_all(sent, ("tm", "ingest"), split_axis=0, concat_axis=0, tiled=True)
    got_rows = got[:, : group_rows * piece_width].reshape(-1, piece_width)
    got_marks = got[:, group_rows * piece_width :].reshape(-1).astype(jnp.int32)
    step_ids = lax.broadcasted_iota(jnp.int32, (1, steps_here), 1)
    onehot = (got_marks[:, None] == step_ids).astype(jnp.bfloat16)
    drive_piece = jnp.einsum("rl,rq->lq", onehot, got_rows, preferred_element_type=jnp.float32)
    partial_force = jnp.einsum("lsq,lq->ls", gain, drive_piece, precision=exact)
    forcing = summed_over(partial_force, "ingest")

    pairs = trans.reshape(steps_here // 2, 2, state_width, state_width)
    level_t = jnp.einsum("jba,jcb->jac", pairs[:, 0], pairs[:, 1], precision=exact)
    while level_t.shape[0] > 1:
        map_pairs = level_t.reshape(-1, 2, state_width, state_width)
        level_t = jnp.einsum("jab,jbc->jac", map_pairs[:, 0], map_pairs[:, 1], precision=exact)
    slab_t = level_t[0]
    offset = run_recurrence(trans, forcing, jnp.zeros((state_width,), jnp.float32))[-1]

    tm_index = lax.axis_index("tm")
    is_first = tm_index == 0
    acc_vec = jnp.where(is_first, jnp.dot(prior_mean, slab_t, precision=exact) + offset, offset)
    acc_t = jnp.where(is_first, jnp.zeros_like(slab_t), slab_t)
    distance = 1
    while distance * 2 < tm_count:
        carried = jnp.concatenate([acc_t, acc_vec[None]], axis=0)
        got = jnp.dot(passed_along(carried, "tm", distance), acc_t, precision=exact)
        acc_t = got[:state_width]
        acc_vec = got[state_width] + acc_vec
        distance *= 2
    previous = passed_along(jnp.concatenate([acc_t, acc_vec[None]], axis=0), "tm", 1)
    before_span = passed_along(acc_vec, "tm", distance + 1)
    entering = jnp.dot(before_span, previous[:state_width], precision=exact) + previous[state_width]
    state = jnp.where(is_first, prior_mean, entering)
    return run_recurrence(trans, forcing, state)


def solution(mesh):
    return jax.shard_map(
        on_device,
        mesh=mesh,
        in_specs=(
            P("tm", None, None),
            P("tm", None, "ingest"),
            P(),
            P(("tm", "ingest"), None),
            P(("tm", "ingest")),
            P(("tm", "ingest")),
            P(("tm", "ingest"), None),
        ),
        out_specs=P("tm", None),
        check_vma=False,
    )
```

```python
import jax
import jax.numpy as jnp
from jax import lax
from jax.experimental import pallas as pl
from jax.experimental.pallas import tpu as pltpu
from jax.sharding import PartitionSpec as P


def passed_along(block, axis, distance):
    devices = range(lax.axis_size(axis))
    route = [(i - distance, i) for i in devices if i - distance in devices]
    return lax.ppermute(block, axis, route)


def summed_over(block, axis):
    count = lax.axis_size(axis)
    shares = [block] + [
        lax.ppermute(block, axis, [(i, (i + shift) % count) for i in range(count)])
        for shift in range(1, count)
    ]
    by_source = jnp.stack(shares)[(lax.axis_index(axis) - jnp.arange(count)) % count]
    total = by_source[0]
    for source in range(1, count):
        total = total + by_source[source]
    return total


def recurrence_kernel(map_ref, force_ref, start_ref, out_ref, state_ref):
    step = pl.program_id(0)

    @pl.when(step == 0)
    def _():
        state_ref[...] = jnp.broadcast_to(start_ref[...], state_ref.shape)

    moved = lax.dot_general(
        state_ref[...],
        map_ref[0],
        (((1,), (1,)), ((), ())),
        precision=lax.Precision.HIGHEST,
        preferred_element_type=jnp.float32,
    )
    state = moved + force_ref[pl.ds(step, 1), :]
    state_ref[...] = state
    out_ref[pl.ds(step, 1), :] = state[0:1, :]


def run_recurrence(trans, forcing, start):
    steps, width = forcing.shape
    return pl.pallas_call(
        recurrence_kernel,
        grid=(steps,),
        in_specs=[
            pl.BlockSpec((1, width, width), lambda t: (t, 0, 0)),
            pl.BlockSpec((steps, width), lambda t: (0, 0)),
            pl.BlockSpec((1, width), lambda t: (0, 0)),
        ],
        out_specs=pl.BlockSpec((steps, width), lambda t: (0, 0)),
        out_shape=jax.ShapeDtypeStruct((steps, width), jnp.float32),
        scratch_shapes=[pltpu.VMEM((8, width), jnp.float32)],
    )(trans, forcing, start.reshape(1, width))


def on_device(
    trans, gain, prior_mean, obs_basis, obs_value, measurement_within_tile, observed_row_count
):
    exact = lax.Precision.HIGHEST
    tm_count = lax.axis_size("tm")
    in_count = lax.axis_size("ingest")
    steps_here = trans.shape[0]
    state_width = trans.shape[1]
    basis_count = obs_basis.shape[1]
    piece_width = basis_count // in_count
    group_rows = obs_basis.shape[0] // tm_count

    weighted = (obs_basis.astype(jnp.float32) * obs_value[:, None]).astype(jnp.bfloat16)
    pieces = weighted.reshape(tm_count, group_rows, in_count, piece_width)
    pieces = pieces.transpose(0, 2, 1, 3).reshape(tm_count * in_count, group_rows * piece_width)
    is_valid = lax.broadcasted_iota(
        jnp.int32, (tm_count, group_rows), 1
    ) < observed_row_count.reshape(tm_count, 1)
    marked = jnp.where(is_valid, measurement_within_tile.reshape(tm_count, group_rows), -1)
    marks = jnp.broadcast_to(
        marked.astype(jnp.bfloat16)[:, None, :], (tm_count, in_count, group_rows)
    ).reshape(tm_count * in_count, group_rows)
    sent = jnp.concatenate([pieces, marks], axis=1)
    got = lax.all_to_all(sent, ("tm", "ingest"), split_axis=0, concat_axis=0, tiled=True)
    got_rows = got[:, : group_rows * piece_width].reshape(-1, piece_width)
    got_marks = got[:, group_rows * piece_width :].reshape(-1).astype(jnp.int32)
    step_ids = lax.broadcasted_iota(jnp.int32, (1, steps_here), 1)
    onehot = (got_marks[:, None] == step_ids).astype(jnp.bfloat16)
    drive_piece = jnp.einsum("rl,rq->lq", onehot, got_rows, preferred_element_type=jnp.float32)
    partial_force = jnp.einsum("lsq,lq->ls", gain, drive_piece, precision=exact)
    forcing = summed_over(partial_force, "ingest")

    pairs = trans.reshape(steps_here // 2, 2, state_width, state_width)
    level_t = jnp.einsum("jba,jcb->jac", pairs[:, 0], pairs[:, 1], precision=exact)
    while level_t.shape[0] > 1:
        map_pairs = level_t.reshape(-1, 2, state_width, state_width)
        level_t = jnp.einsum("jab,jbc->jac", map_pairs[:, 0], map_pairs[:, 1], precision=exact)
    slab_t = level_t[0]
    offset = run_recurrence(trans, forcing, jnp.zeros((state_width,), jnp.float32))[-1]

    tm_index = lax.axis_index("tm")
    is_first = tm_index == 0
    acc_vec = jnp.where(is_first, jnp.dot(prior_mean, slab_t, precision=exact) + offset, offset)
    acc_t = jnp.where(is_first, jnp.zeros_like(slab_t), slab_t)
    got_t = passed_along(acc_t, "tm", 1)
    acc_vec = jnp.dot(passed_along(acc_vec, "tm", 1), acc_t, precision=exact) + acc_vec
    acc_t = jnp.dot(got_t, acc_t, precision=exact)
    distance = 2
    while distance * 2 < tm_count:
        carried = jnp.concatenate([acc_t, acc_vec[None]], axis=0)
        got = jnp.dot(passed_along(carried, "tm", distance), acc_t, precision=exact)
        acc_t = got[:state_width]
        acc_vec = got[state_width] + acc_vec
        distance *= 2
    previous = passed_along(jnp.concatenate([acc_t, acc_vec[None]], axis=0), "tm", 1)
    before_span = passed_along(acc_vec, "tm", distance + 1)
    entering = jnp.dot(before_span, previous[:state_width], precision=exact) + previous[state_width]
    state = jnp.where(is_first, prior_mean, entering)
    return run_recurrence(trans, forcing, state)


def solution(mesh):
    return jax.shard_map(
        on_device,
        mesh=mesh,
        in_specs=(
            P("tm", None, None),
            P("tm", None, "ingest"),
            P(),
            P(("tm", "ingest"), None),
            P(("tm", "ingest")),
            P(("tm", "ingest")),
            P(("tm", "ingest"), None),
        ),
        out_specs=P("tm", None),
        check_vma=False,
    )
```

```python
import jax
import jax.numpy as jnp
from jax import lax
from jax.experimental import pallas as pl
from jax.experimental.pallas import tpu as pltpu
from jax.sharding import PartitionSpec as P


def passed_along(block, axis, distance):
    devices = range(lax.axis_size(axis))
    route = [(i - distance, i) for i in devices if i - distance in devices]
    return lax.ppermute(block, axis, route)


def summed_over(block, axis):
    count = lax.axis_size(axis)
    shares = [block] + [
        lax.ppermute(block, axis, [(i, (i + shift) % count) for i in range(count)])
        for shift in range(1, count)
    ]
    by_source = jnp.stack(shares)[(lax.axis_index(axis) - jnp.arange(count)) % count]
    total = by_source[0]
    for source in range(1, count):
        total = total + by_source[source]
    return total


def recurrence_kernel(map_ref, force_ref, start_ref, out_ref, state_ref):
    step = pl.program_id(0)

    @pl.when(step == 0)
    def _():
        state_ref[...] = jnp.broadcast_to(start_ref[...], state_ref.shape)

    moved = lax.dot_general(
        state_ref[...],
        map_ref[0],
        (((1,), (1,)), ((), ())),
        precision=lax.Precision.HIGH,
        preferred_element_type=jnp.float32,
    )
    state = moved + force_ref[pl.ds(step, 1), :]
    state_ref[...] = state
    out_ref[pl.ds(step, 1), :] = state[0:1, :]


def run_recurrence(trans, forcing, start):
    steps, width = forcing.shape
    return pl.pallas_call(
        recurrence_kernel,
        grid=(steps,),
        in_specs=[
            pl.BlockSpec((1, width, width), lambda t: (t, 0, 0)),
            pl.BlockSpec((steps, width), lambda t: (0, 0)),
            pl.BlockSpec((1, width), lambda t: (0, 0)),
        ],
        out_specs=pl.BlockSpec((steps, width), lambda t: (0, 0)),
        out_shape=jax.ShapeDtypeStruct((steps, width), jnp.float32),
        scratch_shapes=[pltpu.VMEM((8, width), jnp.float32)],
    )(trans, forcing, start.reshape(1, width))


def on_device(
    trans, gain, prior_mean, obs_basis, obs_value, measurement_within_tile, observed_row_count
):
    precise = lax.Precision.HIGH
    tm_count = lax.axis_size("tm")
    in_count = lax.axis_size("ingest")
    steps_here = trans.shape[0]
    state_width = trans.shape[1]
    basis_count = obs_basis.shape[1]
    piece_width = basis_count // in_count
    group_rows = obs_basis.shape[0] // tm_count

    weighted = (obs_basis.astype(jnp.float32) * obs_value[:, None]).astype(jnp.bfloat16)
    pieces = weighted.reshape(tm_count, group_rows, in_count, piece_width)
    pieces = pieces.transpose(0, 2, 1, 3).reshape(tm_count * in_count, group_rows * piece_width)
    is_valid = lax.broadcasted_iota(
        jnp.int32, (tm_count, group_rows), 1
    ) < observed_row_count.reshape(tm_count, 1)
    marked = jnp.where(is_valid, measurement_within_tile.reshape(tm_count, group_rows), -1)
    marks = jnp.broadcast_to(
        marked.astype(jnp.bfloat16)[:, None, :], (tm_count, in_count, group_rows)
    ).reshape(tm_count * in_count, group_rows)
    sent = jnp.concatenate([pieces, marks], axis=1)
    got = lax.all_to_all(sent, ("tm", "ingest"), split_axis=0, concat_axis=0, tiled=True)
    got_rows = got[:, : group_rows * piece_width].reshape(-1, piece_width)
    got_marks = got[:, group_rows * piece_width :].reshape(-1).astype(jnp.int32)
    step_ids = lax.broadcasted_iota(jnp.int32, (1, steps_here), 1)
    onehot = (got_marks[:, None] == step_ids).astype(jnp.bfloat16)
    drive_piece = jnp.einsum("rl,rq->lq", onehot, got_rows, preferred_element_type=jnp.float32)
    partial_force = jnp.einsum("lsq,lq->ls", gain, drive_piece, precision=precise)
    forcing = summed_over(partial_force, "ingest")

    pairs = trans.reshape(steps_here // 2, 2, state_width, state_width)
    level_t = jnp.einsum("jba,jcb->jac", pairs[:, 0], pairs[:, 1], precision=precise)
    while level_t.shape[0] > 1:
        map_pairs = level_t.reshape(-1, 2, state_width, state_width)
        level_t = jnp.einsum("jab,jbc->jac", map_pairs[:, 0], map_pairs[:, 1], precision=precise)
    slab_t = level_t[0]
    offset = run_recurrence(trans, forcing, jnp.zeros((state_width,), jnp.float32))[-1]

    tm_index = lax.axis_index("tm")
    is_first = tm_index == 0
    acc_vec = jnp.where(is_first, jnp.dot(prior_mean, slab_t, precision=precise) + offset, offset)
    acc_t = jnp.where(is_first, jnp.zeros_like(slab_t), slab_t)
    got_t = passed_along(acc_t, "tm", 1)
    acc_vec = jnp.dot(passed_along(acc_vec, "tm", 1), acc_t, precision=precise) + acc_vec
    acc_t = jnp.dot(got_t, acc_t, precision=precise)
    distance = 2
    while distance * 2 < tm_count:
        carried = jnp.concatenate([acc_t, acc_vec[None]], axis=0)
        got = jnp.dot(passed_along(carried, "tm", distance), acc_t, precision=precise)
        acc_t = got[:state_width]
        acc_vec = got[state_width] + acc_vec
        distance *= 2
    previous = passed_along(jnp.concatenate([acc_t, acc_vec[None]], axis=0), "tm", 1)
    before_span = passed_along(acc_vec, "tm", distance + 1)
    entering = jnp.dot(before_span, previous[:state_width], precision=precise) + previous[state_width]
    state = jnp.where(is_first, prior_mean, entering)
    return run_recurrence(trans, forcing, state)


def solution(mesh):
    return jax.shard_map(
        on_device,
        mesh=mesh,
        in_specs=(
            P("tm", None, None),
            P("tm", None, "ingest"),
            P(),
            P(("tm", "ingest"), None),
            P(("tm", "ingest")),
            P(("tm", "ingest")),
            P(("tm", "ingest"), None),
        ),
        out_specs=P("tm", None),
        check_vma=False,
    )
```

```python
import jax
import jax.numpy as jnp
from jax import lax
from jax.experimental import pallas as pl
from jax.experimental.pallas import tpu as pltpu
from jax.sharding import PartitionSpec as P


def passed_along(block, axis, distance):
    devices = range(lax.axis_size(axis))
    route = [(i - distance, i) for i in devices if i - distance in devices]
    return lax.ppermute(block, axis, route)


def sent_to_odd(block, axis, distance):
    devices = range(lax.axis_size(axis))
    route = [(i - distance, i) for i in devices if i % 2 == 1 and i - distance in devices]
    return lax.ppermute(block, axis, route)


def summed_over(block, axis):
    count = lax.axis_size(axis)
    shares = [block] + [
        lax.ppermute(block, axis, [(i, (i + shift) % count) for i in range(count)])
        for shift in range(1, count)
    ]
    by_source = jnp.stack(shares)[(lax.axis_index(axis) - jnp.arange(count)) % count]
    total = by_source[0]
    for source in range(1, count):
        total = total + by_source[source]
    return total


def recurrence_kernel(map_ref, force_ref, start_ref, out_ref, state_ref):
    step = pl.program_id(0)

    @pl.when(step == 0)
    def _():
        state_ref[...] = jnp.broadcast_to(start_ref[...], state_ref.shape)

    moved = lax.dot_general(
        state_ref[...],
        map_ref[0],
        (((1,), (1,)), ((), ())),
        precision=lax.Precision.HIGH,
        preferred_element_type=jnp.float32,
    )
    state = moved + force_ref[pl.ds(step, 1), :]
    state_ref[...] = state
    out_ref[pl.ds(step, 1), :] = state[0:1, :]


def run_recurrence(trans, forcing, start):
    steps, width = forcing.shape
    return pl.pallas_call(
        recurrence_kernel,
        grid=(steps,),
        in_specs=[
            pl.BlockSpec((1, width, width), lambda t: (t, 0, 0)),
            pl.BlockSpec((steps, width), lambda t: (0, 0)),
            pl.BlockSpec((1, width), lambda t: (0, 0)),
        ],
        out_specs=pl.BlockSpec((steps, width), lambda t: (0, 0)),
        out_shape=jax.ShapeDtypeStruct((steps, width), jnp.float32),
        scratch_shapes=[pltpu.VMEM((8, width), jnp.float32)],
    )(trans, forcing, start.reshape(1, width))


def on_device(
    trans, gain, prior_mean, obs_basis, obs_value, measurement_within_tile, observed_row_count
):
    precise = lax.Precision.HIGH
    tm_count = lax.axis_size("tm")
    in_count = lax.axis_size("ingest")
    steps_here = trans.shape[0]
    state_width = trans.shape[1]
    basis_count = obs_basis.shape[1]
    piece_width = basis_count // in_count
    group_rows = obs_basis.shape[0] // tm_count

    weighted = (obs_basis.astype(jnp.float32) * obs_value[:, None]).astype(jnp.bfloat16)
    pieces = weighted.reshape(tm_count, group_rows, in_count, piece_width)
    pieces = pieces.transpose(0, 2, 1, 3).reshape(tm_count * in_count, group_rows * piece_width)
    is_valid = lax.broadcasted_iota(
        jnp.int32, (tm_count, group_rows), 1
    ) < observed_row_count.reshape(tm_count, 1)
    marked = jnp.where(is_valid, measurement_within_tile.reshape(tm_count, group_rows), -1)
    marks = jnp.broadcast_to(
        marked.astype(jnp.bfloat16)[:, None, :], (tm_count, in_count, group_rows)
    ).reshape(tm_count * in_count, group_rows)
    sent = jnp.concatenate([pieces, marks], axis=1)
    got = lax.all_to_all(sent, ("tm", "ingest"), split_axis=0, concat_axis=0, tiled=True)
    got_rows = got[:, : group_rows * piece_width].reshape(-1, piece_width)
    got_marks = got[:, group_rows * piece_width :].reshape(-1).astype(jnp.int32)
    step_ids = lax.broadcasted_iota(jnp.int32, (1, steps_here), 1)
    onehot = (got_marks[:, None] == step_ids).astype(jnp.bfloat16)
    drive_piece = jnp.einsum("rl,rq->lq", onehot, got_rows, preferred_element_type=jnp.float32)
    partial_force = jnp.einsum("lsq,lq->ls", gain, drive_piece, precision=precise)
    forcing = summed_over(partial_force, "ingest")

    pairs = trans.reshape(steps_here // 2, 2, state_width, state_width)
    level_t = jnp.einsum("jba,jcb->jac", pairs[:, 0], pairs[:, 1], precision=precise)
    while level_t.shape[0] > 1:
        map_pairs = level_t.reshape(-1, 2, state_width, state_width)
        level_t = jnp.einsum("jab,jbc->jac", map_pairs[:, 0], map_pairs[:, 1], precision=precise)
    slab_t = level_t[0]
    offset = run_recurrence(trans, forcing, jnp.zeros((state_width,), jnp.float32))[-1]

    tm_index = lax.axis_index("tm")
    is_first = tm_index == 0
    is_odd = tm_index % 2 == 1
    acc_vec = jnp.where(is_first, jnp.dot(prior_mean, slab_t, precision=precise) + offset, offset)
    acc_t = jnp.where(is_first, jnp.zeros_like(slab_t), slab_t)
    pair_t = sent_to_odd(acc_t, "tm", 1)
    pair_vec = sent_to_odd(acc_vec, "tm", 1)
    acc_vec = jnp.dot(pair_vec, acc_t, precision=precise) + acc_vec
    acc_t = jnp.dot(pair_t, acc_t, precision=precise)
    distance = 2
    while distance * 2 < tm_count:
        carried = jnp.concatenate([acc_t, acc_vec[None]], axis=0)
        got = jnp.dot(sent_to_odd(carried, "tm", distance), acc_t, precision=precise)
        acc_t = got[:state_width]
        acc_vec = got[state_width] + acc_vec
        distance *= 2
    acc_vec = jnp.dot(sent_to_odd(acc_vec, "tm", distance), acc_t, precision=precise) + acc_vec
    to_even = lax.ppermute(
        acc_vec, "tm", [(i - 1, i) for i in range(tm_count) if i % 2 == 0 and i >= 1]
    )
    to_odd = sent_to_odd(acc_vec, "tm", 2)
    entering = jnp.where(
        is_odd, jnp.dot(to_odd, pair_t, precision=precise) + pair_vec, to_even
    )
    state = jnp.where(is_first, prior_mean, entering)
    return run_recurrence(trans, forcing, state)


def solution(mesh):
    return jax.shard_map(
        on_device,
        mesh=mesh,
        in_specs=(
            P("tm", None, None),
            P("tm", None, "ingest"),
            P(),
            P(("tm", "ingest"), None),
            P(("tm", "ingest")),
            P(("tm", "ingest")),
            P(("tm", "ingest"), None),
        ),
        out_specs=P("tm", None),
        check_vma=False,
    )
```

```python
import jax
import jax.numpy as jnp
from jax import lax
from jax.experimental import pallas as pl
from jax.experimental.pallas import tpu as pltpu
from jax.sharding import PartitionSpec as P


def passed_along(block, axis, distance):
    devices = range(lax.axis_size(axis))
    route = [(i - distance, i) for i in devices if i - distance in devices]
    return lax.ppermute(block, axis, route)


def sent_to_odd(block, axis, distance):
    devices = range(lax.axis_size(axis))
    route = [(i - distance, i) for i in devices if i % 2 == 1 and i - distance in devices]
    return lax.ppermute(block, axis, route)


def summed_over(block, axis):
    count = lax.axis_size(axis)
    shares = [block] + [
        lax.ppermute(block, axis, [(i, (i + shift) % count) for i in range(count)])
        for shift in range(1, count)
    ]
    by_source = jnp.stack(shares)[(lax.axis_index(axis) - jnp.arange(count)) % count]
    total = by_source[0]
    for source in range(1, count):
        total = total + by_source[source]
    return total


def recurrence_kernel(map_ref, force_ref, start_ref, out_ref, state_ref):
    step = pl.program_id(0)

    @pl.when(step == 0)
    def _():
        state_ref[...] = jnp.broadcast_to(start_ref[...], state_ref.shape)

    moved = lax.dot_general(
        state_ref[...],
        map_ref[0],
        (((1,), (1,)), ((), ())),
        precision=lax.Precision.HIGH,
        preferred_element_type=jnp.float32,
    )
    state = moved + force_ref[pl.ds(step, 1), :]
    state_ref[...] = state
    out_ref[pl.ds(step, 1), :] = state[0:1, :]


def run_recurrence(trans, forcing, start):
    steps, width = forcing.shape
    return pl.pallas_call(
        recurrence_kernel,
        grid=(steps,),
        in_specs=[
            pl.BlockSpec((1, width, width), lambda t: (t, 0, 0)),
            pl.BlockSpec((steps, width), lambda t: (0, 0)),
            pl.BlockSpec((1, width), lambda t: (0, 0)),
        ],
        out_specs=pl.BlockSpec((steps, width), lambda t: (0, 0)),
        out_shape=jax.ShapeDtypeStruct((steps, width), jnp.float32),
        scratch_shapes=[pltpu.VMEM((8, width), jnp.float32)],
    )(trans, forcing, start.reshape(1, width))


def on_device(
    trans, gain, prior_mean, obs_basis, obs_value, measurement_within_tile, observed_row_count
):
    precise = lax.Precision.HIGH
    tm_count = lax.axis_size("tm")
    in_count = lax.axis_size("ingest")
    steps_here = trans.shape[0]
    state_width = trans.shape[1]
    basis_count = obs_basis.shape[1]
    piece_width = basis_count // in_count
    group_rows = obs_basis.shape[0] // tm_count

    weighted = (obs_basis.astype(jnp.float32) * obs_value[:, None]).astype(jnp.bfloat16)
    pieces = weighted.reshape(tm_count, group_rows, in_count, piece_width)
    pieces = pieces.transpose(0, 2, 1, 3).reshape(tm_count * in_count, group_rows * piece_width)
    is_valid = lax.broadcasted_iota(
        jnp.int32, (tm_count, group_rows), 1
    ) < observed_row_count.reshape(tm_count, 1)
    marked = jnp.where(is_valid, measurement_within_tile.reshape(tm_count, group_rows), -1)
    marks = jnp.broadcast_to(
        marked.astype(jnp.bfloat16)[:, None, :], (tm_count, in_count, group_rows)
    ).reshape(tm_count * in_count, group_rows)
    sent = jnp.concatenate([pieces, marks], axis=1)
    got = lax.all_to_all(sent, ("tm", "ingest"), split_axis=0, concat_axis=0, tiled=True)
    pairs = trans.reshape(steps_here // 2, 2, state_width, state_width)
    level_t = jnp.einsum("jba,jcb->jac", pairs[:, 0], pairs[:, 1], precision=precise)
    while level_t.shape[0] > 1:
        map_pairs = level_t.reshape(-1, 2, state_width, state_width)
        level_t = jnp.einsum("jab,jbc->jac", map_pairs[:, 0], map_pairs[:, 1], precision=precise)
    slab_t = level_t[0]
    tm_index = lax.axis_index("tm")
    is_first = tm_index == 0
    is_odd = tm_index % 2 == 1
    slab_first = jnp.where(is_first, jnp.zeros_like(slab_t), slab_t)
    pair_t = sent_to_odd(slab_first, "tm", 1)
    joined_t = jnp.dot(pair_t, slab_first, precision=precise)
    got_t = sent_to_odd(joined_t, "tm", 2)
    got, joined_t = lax.optimization_barrier((got, joined_t))
    acc_t = jnp.dot(got_t, joined_t, precision=precise)
    got_rows = got[:, : group_rows * piece_width].reshape(-1, piece_width)
    got_marks = got[:, group_rows * piece_width :].reshape(-1).astype(jnp.int32)
    step_ids = lax.broadcasted_iota(jnp.int32, (1, steps_here), 1)
    onehot = (got_marks[:, None] == step_ids).astype(jnp.bfloat16)
    drive_piece = jnp.einsum("rl,rq->lq", onehot, got_rows, preferred_element_type=jnp.float32)
    partial_force = jnp.einsum("lsq,lq->ls", gain, drive_piece, precision=precise)
    forcing = summed_over(partial_force, "ingest")

    offset = run_recurrence(trans, forcing, jnp.zeros((state_width,), jnp.float32))[-1]

    acc_vec = jnp.where(is_first, jnp.dot(prior_mean, slab_t, precision=precise) + offset, offset)
    pair_vec = sent_to_odd(acc_vec, "tm", 1)
    acc_vec = jnp.dot(pair_vec, slab_first, precision=precise) + acc_vec
    acc_vec = jnp.dot(sent_to_odd(acc_vec, "tm", 2), joined_t, precision=precise) + acc_vec
    distance = 4
    while distance * 2 < tm_count:
        carried = jnp.concatenate([acc_t, acc_vec[None]], axis=0)
        got = jnp.dot(sent_to_odd(carried, "tm", distance), acc_t, precision=precise)
        acc_t = got[:state_width]
        acc_vec = got[state_width] + acc_vec
        distance *= 2
    acc_vec = jnp.dot(sent_to_odd(acc_vec, "tm", distance), acc_t, precision=precise) + acc_vec
    to_even = lax.ppermute(
        acc_vec, "tm", [(i - 1, i) for i in range(tm_count) if i % 2 == 0 and i >= 1]
    )
    to_odd = sent_to_odd(acc_vec, "tm", 2)
    entering = jnp.where(
        is_odd, jnp.dot(to_odd, pair_t, precision=precise) + pair_vec, to_even
    )
    state = jnp.where(is_first, prior_mean, entering)
    return run_recurrence(trans, forcing, state)


def solution(mesh):
    return jax.shard_map(
        on_device,
        mesh=mesh,
        in_specs=(
            P("tm", None, None),
            P("tm", None, "ingest"),
            P(),
            P(("tm", "ingest"), None),
            P(("tm", "ingest")),
            P(("tm", "ingest")),
            P(("tm", "ingest"), None),
        ),
        out_specs=P("tm", None),
        check_vma=False,
    )
```

```python
import jax
import jax.numpy as jnp
from jax import lax
from jax.experimental import pallas as pl
from jax.experimental.pallas import tpu as pltpu
from jax.sharding import PartitionSpec as P


def passed_along(block, axis, distance):
    devices = range(lax.axis_size(axis))
    route = [(i - distance, i) for i in devices if i - distance in devices]
    return lax.ppermute(block, axis, route)


def sent_to_odd(block, axis, distance):
    devices = range(lax.axis_size(axis))
    route = [(i - distance, i) for i in devices if i % 2 == 1 and i - distance in devices]
    return lax.ppermute(block, axis, route)


def summed_over(block, axis):
    count = lax.axis_size(axis)
    shares = [block] + [
        lax.ppermute(block, axis, [(i, (i + shift) % count) for i in range(count)])
        for shift in range(1, count)
    ]
    by_source = jnp.stack(shares)[(lax.axis_index(axis) - jnp.arange(count)) % count]
    total = by_source[0]
    for source in range(1, count):
        total = total + by_source[source]
    return total


def recurrence_kernel(map_ref, force_ref, start_ref, out_ref, state_ref):
    step = pl.program_id(0)

    @pl.when(step == 0)
    def _():
        state_ref[...] = jnp.broadcast_to(start_ref[...], state_ref.shape)

    moved = lax.dot_general(
        state_ref[...],
        map_ref[0],
        (((1,), (1,)), ((), ())),
        precision=lax.Precision.HIGH,
        preferred_element_type=jnp.float32,
    )
    state = moved + force_ref[pl.ds(step, 1), :]
    state_ref[...] = state
    out_ref[pl.ds(step, 1), :] = state[0:1, :]


def run_recurrence(trans, forcing, start):
    steps, width = forcing.shape
    return pl.pallas_call(
        recurrence_kernel,
        grid=(steps,),
        in_specs=[
            pl.BlockSpec((1, width, width), lambda t: (t, 0, 0)),
            pl.BlockSpec((steps, width), lambda t: (0, 0)),
            pl.BlockSpec((1, width), lambda t: (0, 0)),
        ],
        out_specs=pl.BlockSpec((steps, width), lambda t: (0, 0)),
        out_shape=jax.ShapeDtypeStruct((steps, width), jnp.float32),
        scratch_shapes=[pltpu.VMEM((8, width), jnp.float32)],
    )(trans, forcing, start.reshape(1, width))


def on_device(
    trans, gain, prior_mean, obs_basis, obs_value, measurement_within_tile, observed_row_count
):
    precise = lax.Precision.HIGH
    tm_count = lax.axis_size("tm")
    in_count = lax.axis_size("ingest")
    steps_here = trans.shape[0]
    state_width = trans.shape[1]
    basis_count = obs_basis.shape[1]
    piece_width = basis_count // in_count
    group_rows = obs_basis.shape[0] // tm_count

    weighted = (obs_basis.astype(jnp.float32) * obs_value[:, None]).astype(jnp.bfloat16)
    pieces = weighted.reshape(tm_count, group_rows, in_count, piece_width)
    pieces = pieces.transpose(0, 2, 1, 3).reshape(tm_count * in_count, group_rows * piece_width)
    is_valid = lax.broadcasted_iota(
        jnp.int32, (tm_count, group_rows), 1
    ) < observed_row_count.reshape(tm_count, 1)
    marked = jnp.where(is_valid, measurement_within_tile.reshape(tm_count, group_rows), -1)
    marks = jnp.broadcast_to(
        marked.astype(jnp.bfloat16)[:, None, :], (tm_count, in_count, group_rows)
    ).reshape(tm_count * in_count, group_rows)
    sent = jnp.concatenate([pieces, marks], axis=1)
    got = lax.all_to_all(sent, ("tm", "ingest"), split_axis=0, concat_axis=0, tiled=True)
    pairs = trans.reshape(steps_here // 2, 2, state_width, state_width)
    level_t = jnp.einsum("jba,jcb->jac", pairs[:, 0], pairs[:, 1], precision=precise)
    while level_t.shape[0] > 1:
        map_pairs = level_t.reshape(-1, 2, state_width, state_width)
        level_t = jnp.einsum("jab,jbc->jac", map_pairs[:, 0], map_pairs[:, 1], precision=precise)
    slab_t = level_t[0]
    tm_index = lax.axis_index("tm")
    is_first = tm_index == 0
    is_odd = tm_index % 2 == 1
    slab_first = jnp.where(is_first, jnp.zeros_like(slab_t), slab_t)
    pair_t = sent_to_odd(slab_first, "tm", 1)
    joined_t = jnp.dot(pair_t, slab_first, precision=precise)
    got_t = sent_to_odd(joined_t, "tm", 2)
    acc_t = jnp.dot(got_t, joined_t, precision=precise)
    got_rows = got[:, : group_rows * piece_width].reshape(-1, piece_width)
    got_marks = got[:, group_rows * piece_width :].reshape(-1).astype(jnp.int32)
    step_ids = lax.broadcasted_iota(jnp.int32, (1, steps_here), 1)
    onehot = (got_marks[:, None] == step_ids).astype(jnp.bfloat16)
    drive_piece = jnp.einsum("rl,rq->lq", onehot, got_rows, preferred_element_type=jnp.float32)
    partial_force = jnp.einsum("lsq,lq->ls", gain, drive_piece, precision=precise)
    partial_force, joined_t = lax.optimization_barrier((partial_force, joined_t))
    forcing = summed_over(partial_force, "ingest")

    offset = run_recurrence(trans, forcing, jnp.zeros((state_width,), jnp.float32))[-1]

    acc_vec = jnp.where(is_first, jnp.dot(prior_mean, slab_t, precision=precise) + offset, offset)
    pair_vec = sent_to_odd(acc_vec, "tm", 1)
    acc_vec = jnp.dot(pair_vec, slab_first, precision=precise) + acc_vec
    acc_vec = jnp.dot(sent_to_odd(acc_vec, "tm", 2), joined_t, precision=precise) + acc_vec
    distance = 4
    while distance * 2 < tm_count:
        carried = jnp.concatenate([acc_t, acc_vec[None]], axis=0)
        got = jnp.dot(sent_to_odd(carried, "tm", distance), acc_t, precision=precise)
        acc_t = got[:state_width]
        acc_vec = got[state_width] + acc_vec
        distance *= 2
    acc_vec = jnp.dot(sent_to_odd(acc_vec, "tm", distance), acc_t, precision=precise) + acc_vec
    to_even = lax.ppermute(
        acc_vec, "tm", [(i - 1, i) for i in range(tm_count) if i % 2 == 0 and i >= 1]
    )
    to_odd = sent_to_odd(acc_vec, "tm", 2)
    entering = jnp.where(
        is_odd, jnp.dot(to_odd, pair_t, precision=precise) + pair_vec, to_even
    )
    state = jnp.where(is_first, prior_mean, entering)
    return run_recurrence(trans, forcing, state)


def solution(mesh):
    return jax.shard_map(
        on_device,
        mesh=mesh,
        in_specs=(
            P("tm", None, None),
            P("tm", None, "ingest"),
            P(),
            P(("tm", "ingest"), None),
            P(("tm", "ingest")),
            P(("tm", "ingest")),
            P(("tm", "ingest"), None),
        ),
        out_specs=P("tm", None),
        check_vma=False,
    )
```

```python
import jax
import jax.numpy as jnp
from jax import lax
from jax.experimental import pallas as pl
from jax.experimental.pallas import tpu as pltpu
from jax.sharding import PartitionSpec as P


def passed_along(block, axis, distance):
    devices = range(lax.axis_size(axis))
    route = [(i - distance, i) for i in devices if i - distance in devices]
    return lax.ppermute(block, axis, route)


def sent_to_odd(block, axis, distance):
    devices = range(lax.axis_size(axis))
    route = [(i - distance, i) for i in devices if i % 2 == 1 and i - distance in devices]
    return lax.ppermute(block, axis, route)


def summed_over(block, axis):
    count = lax.axis_size(axis)
    shares = [block] + [
        lax.ppermute(block, axis, [(i, (i + shift) % count) for i in range(count)])
        for shift in range(1, count)
    ]
    by_source = jnp.stack(shares)[(lax.axis_index(axis) - jnp.arange(count)) % count]
    total = by_source[0]
    for source in range(1, count):
        total = total + by_source[source]
    return total


def recurrence_kernel(map_ref, force_ref, start_ref, out_ref):
    state = jnp.broadcast_to(start_ref[...], (8, start_ref.shape[1]))
    for step in range(map_ref.shape[0]):
        moved = lax.dot_general(
            state,
            map_ref[step],
            (((1,), (1,)), ((), ())),
            precision=lax.Precision.HIGH,
            preferred_element_type=jnp.float32,
        )
        state = moved + force_ref[step : step + 1, :]
        out_ref[step : step + 1, :] = state[0:1, :]


def run_recurrence(trans, forcing, start):
    steps, width = forcing.shape
    return pl.pallas_call(
        recurrence_kernel,
        out_shape=jax.ShapeDtypeStruct((steps, width), jnp.float32),
    )(trans, forcing, start.reshape(1, width))


def sent_to_odd(block, axis, distance):
    devices = range(lax.axis_size(axis))
    route = [(i - distance, i) for i in devices if i % 2 == 1 and i - distance in devices]
    return lax.ppermute(block, axis, route)


def summed_over(block, axis):
    count = lax.axis_size(axis)
    shares = [block] + [
        lax.ppermute(block, axis, [(i, (i + shift) % count) for i in range(count)])
        for shift in range(1, count)
    ]
    by_source = jnp.stack(shares)[(lax.axis_index(axis) - jnp.arange(count)) % count]
    total = by_source[0]
    for source in range(1, count):
        total = total + by_source[source]
    return total


def recurrence_kernel(map_ref, force_ref, start_ref, out_ref, state_ref):
    step = pl.program_id(0)

    @pl.when(step == 0)
    def _():
        state_ref[...] = jnp.broadcast_to(start_ref[...], state_ref.shape)

    moved = lax.dot_general(
        state_ref[...],
        map_ref[0],
        (((1,), (1,)), ((), ())),
        precision=lax.Precision.HIGH,
        preferred_element_type=jnp.float32,
    )
    state = moved + force_ref[pl.ds(step, 1), :]
    state_ref[...] = state
    out_ref[pl.ds(step, 1), :] = state[0:1, :]


def run_recurrence(trans, forcing, start):
    steps, width = forcing.shape
    return pl.pallas_call(
        recurrence_kernel,
        grid=(steps,),
        in_specs=[
            pl.BlockSpec((1, width, width), lambda t: (t, 0, 0)),
            pl.BlockSpec((steps, width), lambda t: (0, 0)),
            pl.BlockSpec((1, width), lambda t: (0, 0)),
        ],
        out_specs=pl.BlockSpec((steps, width), lambda t: (0, 0)),
        out_shape=jax.ShapeDtypeStruct((steps, width), jnp.float32),
        scratch_shapes=[pltpu.VMEM((8, width), jnp.float32)],
    )(trans, forcing, start.reshape(1, width))


def on_device(
    trans, gain, prior_mean, obs_basis, obs_value, measurement_within_tile, observed_row_count
):
    precise = lax.Precision.HIGH
    tm_count = lax.axis_size("tm")
    in_count = lax.axis_size("ingest")
    steps_here = trans.shape[0]
    state_width = trans.shape[1]
    basis_count = obs_basis.shape[1]
    piece_width = basis_count // in_count
    group_rows = obs_basis.shape[0] // tm_count

    weighted = (obs_basis.astype(jnp.float32) * obs_value[:, None]).astype(jnp.bfloat16)
    pieces = weighted.reshape(tm_count, group_rows, in_count, piece_width)
    pieces = pieces.transpose(0, 2, 1, 3).reshape(tm_count * in_count, group_rows * piece_width)
    is_valid = lax.broadcasted_iota(
        jnp.int32, (tm_count, group_rows), 1
    ) < observed_row_count.reshape(tm_count, 1)
    marked = jnp.where(is_valid, measurement_within_tile.reshape(tm_count, group_rows), -1)
    marks = jnp.broadcast_to(
        marked.astype(jnp.bfloat16)[:, None, :], (tm_count, in_count, group_rows)
    ).reshape(tm_count * in_count, group_rows)
    sent = jnp.concatenate([pieces, marks], axis=1)
    got = lax.all_to_all(sent, ("tm", "ingest"), split_axis=0, concat_axis=0, tiled=True)
    pairs = trans.reshape(steps_here // 2, 2, state_width, state_width)
    level_t = jnp.einsum("jba,jcb->jac", pairs[:, 0], pairs[:, 1], precision=precise)
    while level_t.shape[0] > 1:
        map_pairs = level_t.reshape(-1, 2, state_width, state_width)
        level_t = jnp.einsum("jab,jbc->jac", map_pairs[:, 0], map_pairs[:, 1], precision=precise)
    slab_t = level_t[0]
    tm_index = lax.axis_index("tm")
    is_first = tm_index == 0
    is_odd = tm_index % 2 == 1
    slab_first = jnp.where(is_first, jnp.zeros_like(slab_t), slab_t)
    pair_t = sent_to_odd(slab_first, "tm", 1)
    joined_t = jnp.dot(pair_t, slab_first, precision=precise)
    got_t = sent_to_odd(joined_t, "tm", 2)
    acc_t = jnp.dot(got_t, joined_t, precision=precise)
    got_rows = got[:, : group_rows * piece_width].reshape(-1, piece_width)
    got_marks = got[:, group_rows * piece_width :].reshape(-1).astype(jnp.int32)
    step_ids = lax.broadcasted_iota(jnp.int32, (1, steps_here), 1)
    onehot = (got_marks[:, None] == step_ids).astype(jnp.bfloat16)
    drive_piece = jnp.einsum("rl,rq->lq", onehot, got_rows, preferred_element_type=jnp.float32)
    partial_force = jnp.einsum("lsq,lq->ls", gain, drive_piece, precision=precise)
    partial_force, joined_t = lax.optimization_barrier((partial_force, joined_t))
    forcing = summed_over(partial_force, "ingest")

    offset = run_recurrence(trans, forcing, jnp.zeros((state_width,), jnp.float32))[-1]

    acc_vec = jnp.where(is_first, jnp.dot(prior_mean, slab_t, precision=precise) + offset, offset)
    pair_vec = sent_to_odd(acc_vec, "tm", 1)
    acc_vec = jnp.dot(pair_vec, slab_first, precision=precise) + acc_vec
    acc_vec = jnp.dot(sent_to_odd(acc_vec, "tm", 2), joined_t, precision=precise) + acc_vec
    distance = 4
    while distance * 2 < tm_count:
        carried = jnp.concatenate([acc_t, acc_vec[None]], axis=0)
        got = jnp.dot(sent_to_odd(carried, "tm", distance), acc_t, precision=precise)
        acc_t = got[:state_width]
        acc_vec = got[state_width] + acc_vec
        distance *= 2
    acc_vec = jnp.dot(sent_to_odd(acc_vec, "tm", distance), acc_t, precision=precise) + acc_vec
    to_even = lax.ppermute(
        acc_vec, "tm", [(i - 1, i) for i in range(tm_count) if i % 2 == 0 and i >= 1]
    )
    to_odd = sent_to_odd(acc_vec, "tm", 2)
    entering = jnp.where(
        is_odd, jnp.dot(to_odd, pair_t, precision=precise) + pair_vec, to_even
    )
    state = jnp.where(is_first, prior_mean, entering)
    return run_recurrence(trans, forcing, state)


def solution(mesh):
    return jax.shard_map(
        on_device,
        mesh=mesh,
        in_specs=(
            P("tm", None, None),
            P("tm", None, "ingest"),
            P(),
            P(("tm", "ingest"), None),
            P(("tm", "ingest")),
            P(("tm", "ingest")),
            P(("tm", "ingest"), None),
        ),
        out_specs=P("tm", None),
        check_vma=False,
    )
```
